128 devices in a mesh: prow: 16 (over x, y), pcol: 8 (over z, core).
Axes of the slice: x: 4, y: 4, z: 4, core: 2. Of those that a mesh axis runs over, the one named last changes fastest.
Arguments:
- block: float32 [32768, 10240], P('prow', 'pcol'), may hold values from -6 to 6
Outputs:
- top: float32 [256, 10240], P(None, 'pcol')
- updated: float32 [32768, 10240], P('prow', 'pcol')
The draws below stay inside these ranges and needn't reach their ends.
All inputs are finite; a program needn't handle non-finite values.
Results may differ from the reference program's by a relative error of at most 0.000073.
Values sent between devices are 32-bit elements; how exact they have to be, the bound alone decides.
No kernel may reach another device: no remote copies, remote signals or barrier semaphores. Data moves between devices by JAX's collectives and lax.ppermute only.
A program may use at most 128 MiB of HBM per device.

```python
import jax
import jax.numpy as jnp
from jax import lax

NB = 256
MROWS = 32768
NCOL = 10240


def block_levels(stream_key, dims, shards, smallest, top_value):
    def one(dim, parts):
        steps = jax.random.uniform(jax.random.fold_in(jax.random.fold_in(stream_key, 6), dim), (parts,), jnp.float32, smallest / len(shards), top_value / len(shards))
        return jnp.repeat(jnp.exp(steps), dims[dim] // parts).reshape((-1,) + (1,) * (len(dims) - dim - 1))

    gain = one(*shards[0])
    for cut in shards[1:]:
        gain = gain * one(*cut)
    return gain


def centred(key, extent, scale, reach, shards=(), kind=jnp.bfloat16):
    gain = block_levels(key, extent, shards, -0.22, 0.18) if shards else 1.0
    result = jax.random.normal(key, extent, jnp.float32) * scale * gain
    return jnp.minimum(jnp.maximum(result, -reach), reach).astype(kind)


def setup_inputs(seed: int = 0) -> dict:
    keys = jax.random.split(jax.random.key(seed), 2)
    block = centred(keys[0], (MROWS, NCOL), 1.0, 6.0, ((0, 16), (1, 8)), jnp.float32)
    return dict(block=block)


def solve_triangular(matrix, right, lower):
    return jax.scipy.linalg.solve_triangular(matrix, right, lower=lower)

def reference(block):
    highest = lax.Precision.HIGHEST
    panel = block[:, :NB]
    gram = jnp.dot(panel.T.astype(jnp.float32), panel.astype(jnp.float32), precision=highest, preferred_element_type=jnp.float32)
    factor = jnp.linalg.cholesky(gram)
    products = jnp.dot(panel.T.astype(jnp.float32), block.astype(jnp.float32), precision=highest, preferred_element_type=jnp.float32)
    top = solve_triangular(factor, products, True)
    basis = solve_triangular(factor, panel.T, True).T
    rest = block[:, NB:] - jnp.dot(basis.astype(jnp.float32), top[:, NB:].astype(jnp.float32), precision=highest, preferred_element_type=jnp.float32)
    updated = jnp.concatenate([basis, rest], axis=1)
    return (top, updated)
```

```python
import jax
import jax.numpy as jnp
from jax import lax
from jax.sharding import PartitionSpec as P

NB = 256
HIGHEST = lax.Precision.HIGHEST


def a2a_allreduce(value, axis, size):
    rows = value.shape[0]
    pieces = value.reshape(size, rows // size, *value.shape[1:])
    mine = lax.all_to_all(pieces, axis, 0, 0).sum(0)
    spread = jnp.broadcast_to(mine[None], (size,) + mine.shape)
    return lax.all_to_all(spread, axis, 0, 0).reshape(value.shape)


def a2a_broadcast(value, axis, size):
    rows = value.shape[0]
    pieces = value.reshape(size, rows // size, *value.shape[1:])
    mine = lax.all_to_all(pieces, axis, 0, 0)[0]
    spread = jnp.broadcast_to(mine[None], (size,) + mine.shape)
    return lax.all_to_all(spread, axis, 0, 0).reshape(value.shape)


def inner(left, right):
    return lax.dot_general(
        left, right, (((0,), (0,)), ((), ())),
        precision=HIGHEST, preferred_element_type=jnp.float32,
    )


def body(block, nrow, ncol):
    cols_here = block.shape[1]
    panel = a2a_broadcast(block[:, :NB], "pcol", ncol)
    sums = a2a_allreduce(
        jnp.concatenate([inner(panel, panel), inner(panel, block)], axis=1), "prow", nrow
    )
    gram, products = sums[:, :NB], sums[:, NB:]
    factor = jnp.linalg.cholesky(gram)
    top = lax.linalg.triangular_solve(factor, products, left_side=True, lower=True)
    basis = lax.linalg.triangular_solve(
        factor, panel, left_side=False, lower=True, transpose_a=True
    )
    rest = block - jnp.dot(basis, top, precision=HIGHEST, preferred_element_type=jnp.float32)
    widened = jnp.pad(basis, ((0, 0), (0, cols_here - NB)))
    column_ids = lax.axis_index("pcol") * cols_here + jnp.arange(cols_here, dtype=jnp.int32)
    updated = jnp.where((column_ids < NB)[None, :], widened, rest)
    return (top, updated)


def solution(mesh):
    nrow, ncol = mesh.shape["prow"], mesh.shape["pcol"]
    placed = (P("prow", "pcol"),)
    return jax.shard_map(
        lambda b: body(b, nrow, ncol),
        mesh=mesh,
        in_specs=placed,
        out_specs=(P(None, "pcol"), P("prow", "pcol")),
        check_vma=False,
    )
```

```python
import jax
import jax.numpy as jnp
from jax import lax
from jax.sharding import PartitionSpec as P

NB = 256
HIGHEST = lax.Precision.HIGHEST


def a2a_allreduce(value, axis, size):
    rows = value.shape[0]
    pieces = value.reshape(size, rows // size, *value.shape[1:])
    mine = lax.all_to_all(pieces, axis, 0, 0).sum(0)
    spread = jnp.broadcast_to(mine[None], (size,) + mine.shape)
    return lax.all_to_all(spread, axis, 0, 0).reshape(value.shape)


def a2a_broadcast(value, axis, size):
    rows = value.shape[0]
    pieces = value.reshape(size, rows // size, *value.shape[1:])
    mine = lax.all_to_all(pieces, axis, 0, 0)[0]
    spread = jnp.broadcast_to(mine[None], (size,) + mine.shape)
    return lax.all_to_all(spread, axis, 0, 0).reshape(value.shape)


def inner(left, right):
    return lax.dot_general(
        left, right, (((0,), (0,)), ((), ())),
        precision=HIGHEST, preferred_element_type=jnp.float32,
    )


def body(block, nrow, ncol):
    cols_here = block.shape[1]
    own = block[:, :NB]
    gram = a2a_allreduce(inner(own, own), "prow", nrow)
    got = a2a_broadcast(jnp.concatenate([own, gram], axis=0), "pcol", ncol)
    panel, gram = got[: own.shape[0]], got[own.shape[0]:]
    factor = jnp.linalg.cholesky(gram)
    products = a2a_allreduce(inner(panel, block), "prow", nrow)
    top = lax.linalg.triangular_solve(factor, products, left_side=True, lower=True)
    basis = lax.linalg.triangular_solve(
        factor, panel, left_side=False, lower=True, transpose_a=True
    )
    rest = block - jnp.dot(basis, top, precision=HIGHEST, preferred_element_type=jnp.float32)
    widened = jnp.pad(basis, ((0, 0), (0, cols_here - NB)))
    column_ids = lax.axis_index("pcol") * cols_here + jnp.arange(cols_here, dtype=jnp.int32)
    updated = jnp.where((column_ids < NB)[None, :], widened, rest)
    return (top, updated)


def solution(mesh):
    nrow, ncol = mesh.shape["prow"], mesh.shape["pcol"]
    placed = (P("prow", "pcol"),)
    return jax.shard_map(
        lambda b: body(b, nrow, ncol),
        mesh=mesh,
        in_specs=placed,
        out_specs=(P(None, "pcol"), P("prow", "pcol")),
        check_vma=False,
    )
```

```python
import jax
import jax.numpy as jnp
from jax import lax
from jax.sharding import PartitionSpec as P

NB = 256
HIGHEST = lax.Precision.HIGHEST


def a2a_allreduce(value, axis, size):
    rows = value.shape[0]
    pieces = value.reshape(size, rows // size, *value.shape[1:])
    mine = lax.all_to_all(pieces, axis, 0, 0).sum(0)
    spread = jnp.broadcast_to(mine[None], (size,) + mine.shape)
    return lax.all_to_all(spread, axis, 0, 0).reshape(value.shape)


def a2a_broadcast(value, axis, size):
    rows = value.shape[0]
    pieces = value.reshape(size, rows // size, *value.shape[1:])
    mine = lax.all_to_all(pieces, axis, 0, 0)[0]
    spread = jnp.broadcast_to(mine[None], (size,) + mine.shape)
    return lax.all_to_all(spread, axis, 0, 0).reshape(value.shape)


def inner(left, right):
    return lax.dot_general(
        left, right, (((0,), (0,)), ((), ())),
        precision=HIGHEST, preferred_element_type=jnp.float32,
    )


def mm(left, right):
    return jnp.dot(left, right, precision=HIGHEST, preferred_element_type=jnp.float32)


def lower_inverse(block):
    eye = jnp.eye(block.shape[0], dtype=block.dtype)
    return lax.linalg.triangular_solve(block, eye, left_side=True, lower=True)


def inverse_factor(gram):
    half = gram.shape[0] // 2
    l11 = jnp.linalg.cholesky(gram[:half, :half])
    i11 = lower_inverse(l11)
    l21 = lax.dot_general(
        gram[half:, :half], i11, (((1,), (1,)), ((), ())),
        precision=HIGHEST, preferred_element_type=jnp.float32,
    )
    schur = gram[half:, half:] - lax.dot_general(
        l21, l21, (((1,), (1,)), ((), ())),
        precision=HIGHEST, preferred_element_type=jnp.float32,
    )
    l22 = jnp.linalg.cholesky(schur)
    i22 = lower_inverse(l22)
    i21 = -mm(mm(i22, l21), i11)
    zeros = jnp.zeros((half, gram.shape[0] - half), gram.dtype)
    return jnp.concatenate(
        [jnp.concatenate([i11, zeros], axis=1), jnp.concatenate([i21, i22], axis=1)], axis=0
    )


def body(block, nrow, ncol):
    cols_here = block.shape[1]
    own = block[:, :NB]
    gram = a2a_allreduce(inner(own, own), "prow", nrow)
    got = a2a_broadcast(jnp.concatenate([own, gram], axis=0), "pcol", ncol)
    panel, gram = got[: own.shape[0]], got[own.shape[0]:]
    inv = inverse_factor(gram)
    products = a2a_allreduce(inner(panel, block), "prow", nrow)
    top = mm(inv, products)
    basis = lax.dot_general(
        panel, inv, (((1,), (1,)), ((), ())),
        precision=HIGHEST, preferred_element_type=jnp.float32,
    )
    rest = block - jnp.dot(basis, top, precision=HIGHEST, preferred_element_type=jnp.float32)
    widened = jnp.pad(basis, ((0, 0), (0, cols_here - NB)))
    column_ids = lax.axis_index("pcol") * cols_here + jnp.arange(cols_here, dtype=jnp.int32)
    updated = jnp.where((column_ids < NB)[None, :], widened, rest)
    return (top, updated)


def solution(mesh):
    nrow, ncol = mesh.shape["prow"], mesh.shape["pcol"]
    placed = (P("prow", "pcol"),)
    return jax.shard_map(
        lambda b: body(b, nrow, ncol),
        mesh=mesh,
        in_specs=placed,
        out_specs=(P(None, "pcol"), P("prow", "pcol")),
        check_vma=False,
    )
```

```python
import jax
import jax.numpy as jnp
from jax import lax
from jax.sharding import PartitionSpec as P

NB = 256
HIGHEST = lax.Precision.HIGHEST


def a2a_allreduce(value, axis, size):
    rows = value.shape[0]
    pieces = value.reshape(size, rows // size, *value.shape[1:])
    mine = lax.all_to_all(pieces, axis, 0, 0).sum(0)
    spread = jnp.broadcast_to(mine[None], (size,) + mine.shape)
    return lax.all_to_all(spread, axis, 0, 0).reshape(value.shape)


def a2a_broadcast(value, axis, size):
    rows = value.shape[0]
    pieces = value.reshape(size, rows // size, *value.shape[1:])
    mine = lax.all_to_all(pieces, axis, 0, 0)[0]
    spread = jnp.broadcast_to(mine[None], (size,) + mine.shape)
    return lax.all_to_all(spread, axis, 0, 0).reshape(value.shape)


def tree_broadcast(value, axis):
    me = lax.axis_index(axis)
    value = jnp.where(me == 0, value, 0).astype(value.dtype)
    value = value + lax.ppermute(value, axis, [(0, 1)])
    value = value + lax.ppermute(value, axis, [(0, 2), (1, 7)])
    far = lax.ppermute(value, axis, [(2, 4), (7, 5)])
    near = lax.ppermute(value, axis, [(2, 3), (7, 6)])
    return value + far + near


def inner(left, right):
    return lax.dot_general(
        left, right, (((0,), (0,)), ((), ())),
        precision=HIGHEST, preferred_element_type=jnp.float32,
    )


def mm(left, right):
    return jnp.dot(left, right, precision=HIGHEST, preferred_element_type=jnp.float32)


def lower_inverse(block):
    eye = jnp.eye(block.shape[0], dtype=block.dtype)
    return lax.linalg.triangular_solve(block, eye, left_side=True, lower=True)


def inverse_factor(gram):
    half = gram.shape[0] // 2
    l11 = jnp.linalg.cholesky(gram[:half, :half])
    i11 = lower_inverse(l11)
    l21 = lax.dot_general(
        gram[half:, :half], i11, (((1,), (1,)), ((), ())),
        precision=HIGHEST, preferred_element_type=jnp.float32,
    )
    schur = gram[half:, half:] - lax.dot_general(
        l21, l21, (((1,), (1,)), ((), ())),
        precision=HIGHEST, preferred_element_type=jnp.float32,
    )
    l22 = jnp.linalg.cholesky(schur)
    i22 = lower_inverse(l22)
    i21 = -mm(mm(i22, l21), i11)
    zeros = jnp.zeros((half, gram.shape[0] - half), gram.dtype)
    return jnp.concatenate(
        [jnp.concatenate([i11, zeros], axis=1), jnp.concatenate([i21, i22], axis=1)], axis=0
    )


def body(block, nrow, ncol):
    cols_here = block.shape[1]
    own = block[:, :NB]
    if ncol == 8:
        panel = tree_broadcast(own, "pcol")
        gram = tree_broadcast(a2a_allreduce(inner(own, own), "prow", nrow), "pcol")
    else:
        gram = a2a_allreduce(inner(own, own), "prow", nrow)
        got = a2a_broadcast(jnp.concatenate([own, gram], axis=0), "pcol", ncol)
        panel, gram = got[: own.shape[0]], got[own.shape[0]:]
    inv = inverse_factor(gram)
    products = a2a_allreduce(inner(panel, block), "prow", nrow)
    top = mm(inv, products)
    basis = lax.dot_general(
        panel, inv, (((1,), (1,)), ((), ())),
        precision=HIGHEST, preferred_element_type=jnp.float32,
    )
    rest = block - jnp.dot(basis, top, precision=HIGHEST, preferred_element_type=jnp.float32)
    widened = jnp.pad(basis, ((0, 0), (0, cols_here - NB)))
    column_ids = lax.axis_index("pcol") * cols_here + jnp.arange(cols_here, dtype=jnp.int32)
    updated = jnp.where((column_ids < NB)[None, :], widened, rest)
    return (top, updated)


def solution(mesh):
    nrow, ncol = mesh.shape["prow"], mesh.shape["pcol"]
    placed = (P("prow", "pcol"),)
    return jax.shard_map(
        lambda b: body(b, nrow, ncol),
        mesh=mesh,
        in_specs=placed,
        out_specs=(P(None, "pcol"), P("prow", "pcol")),
        check_vma=False,
    )
```

```python
import jax
import jax.numpy as jnp
from jax import lax
from jax.sharding import PartitionSpec as P

NB = 256
HIGHEST = lax.Precision.HIGHEST
HIGH = lax.Precision.HIGH


def a2a_allreduce(value, axis, size):
    rows = value.shape[0]
    pieces = value.reshape(size, rows // size, *value.shape[1:])
    mine = lax.all_to_all(pieces, axis, 0, 0).sum(0)
    spread = jnp.broadcast_to(mine[None], (size,) + mine.shape)
    return lax.all_to_all(spread, axis, 0, 0).reshape(value.shape)


def a2a_broadcast(value, axis, size):
    rows = value.shape[0]
    pieces = value.reshape(size, rows // size, *value.shape[1:])
    mine = lax.all_to_all(pieces, axis, 0, 0)[0]
    spread = jnp.broadcast_to(mine[None], (size,) + mine.shape)
    return lax.all_to_all(spread, axis, 0, 0).reshape(value.shape)


def tree_broadcast(value, axis):
    me = lax.axis_index(axis)
    value = jnp.where(me == 0, value, 0).astype(value.dtype)
    value = value + lax.ppermute(value, axis, [(0, 1)])
    value = value + lax.ppermute(value, axis, [(0, 2), (1, 7)])
    far = lax.ppermute(value, axis, [(2, 4), (7, 5)])
    near = lax.ppermute(value, axis, [(2, 3), (7, 6)])
    return value + far + near


def inner(left, right, precision=HIGHEST):
    return lax.dot_general(
        left, right, (((0,), (0,)), ((), ())),
        precision=precision, preferred_element_type=jnp.float32,
    )


def mm(left, right):
    return jnp.dot(left, right, precision=HIGHEST, preferred_element_type=jnp.float32)


def lower_inverse(block):
    eye = jnp.eye(block.shape[0], dtype=block.dtype)
    return lax.linalg.triangular_solve(block, eye, left_side=True, lower=True)


def inverse_factor(gram):
    half = gram.shape[0] // 2
    l11 = lax.linalg.cholesky(gram[:half, :half], symmetrize_input=False)
    i11 = lower_inverse(l11)
    l21 = lax.dot_general(
        gram[half:, :half], i11, (((1,), (1,)), ((), ())),
        precision=HIGHEST, preferred_element_type=jnp.float32,
    )
    schur = gram[half:, half:] - lax.dot_general(
        l21, l21, (((1,), (1,)), ((), ())),
        precision=HIGHEST, preferred_element_type=jnp.float32,
    )
    l22 = lax.linalg.cholesky(schur, symmetrize_input=False)
    i22 = lower_inverse(l22)
    i21 = -mm(mm(i22, l21), i11)
    zeros = jnp.zeros((half, gram.shape[0] - half), gram.dtype)
    return jnp.concatenate(
        [jnp.concatenate([i11, zeros], axis=1), jnp.concatenate([i21, i22], axis=1)], axis=0
    )


def body(block, nrow, ncol):
    cols_here = block.shape[1]
    own = block[:, :NB]
    if ncol == 8:
        panel = tree_broadcast(own, "pcol")
        gram = tree_broadcast(a2a_allreduce(inner(own, own), "prow", nrow), "pcol")
    else:
        gram = a2a_allreduce(inner(own, own), "prow", nrow)
        got = a2a_broadcast(jnp.concatenate([own, gram], axis=0), "pcol", ncol)
        panel, gram = got[: own.shape[0]], got[own.shape[0]:]
    inv = inverse_factor(gram)
    products = a2a_allreduce(inner(panel, block, HIGH), "prow", nrow)
    top = mm(inv, products)
    basis = lax.dot_general(
        panel, inv, (((1,), (1,)), ((), ())),
        precision=HIGHEST, preferred_element_type=jnp.float32,
    )
    rest = block - jnp.dot(basis, top, precision=HIGH, preferred_element_type=jnp.float32)
    widened = jnp.pad(basis, ((0, 0), (0, cols_here - NB)))
    column_ids = lax.axis_index("pcol") * cols_here + jnp.arange(cols_here, dtype=jnp.int32)
    updated = jnp.where((column_ids < NB)[None, :], widened, rest)
    return (top, updated)


def solution(mesh):
    nrow, ncol = mesh.shape["prow"], mesh.shape["pcol"]
    placed = (P("prow", "pcol"),)
    return jax.shard_map(
        lambda b: body(b, nrow, ncol),
        mesh=mesh,
        in_specs=placed,
        out_specs=(P(None, "pcol"), P("prow", "pcol")),
        check_vma=False,
    )
```

```python
import jax
import jax.numpy as jnp
from jax import lax
from jax.sharding import PartitionSpec as P

NB = 256
HIGHEST = lax.Precision.HIGHEST
HIGH = lax.Precision.HIGH


def a2a_allreduce(value, axis, size):
    rows = value.shape[0]
    pieces = value.reshape(size, rows // size, *value.shape[1:])
    mine = lax.all_to_all(pieces, axis, 0, 0).sum(0)
    spread = jnp.broadcast_to(mine[None], (size,) + mine.shape)
    return lax.all_to_all(spread, axis, 0, 0).reshape(value.shape)


def a2a_broadcast(value, axis, size):
    rows = value.shape[0]
    pieces = value.reshape(size, rows // size, *value.shape[1:])
    mine = lax.all_to_all(pieces, axis, 0, 0)[0]
    spread = jnp.broadcast_to(mine[None], (size,) + mine.shape)
    return lax.all_to_all(spread, axis, 0, 0).reshape(value.shape)


def tree_broadcast(value, axis):
    me = lax.axis_index(axis)
    value = jnp.where(me == 0, value, 0).astype(value.dtype)
    value = value + lax.ppermute(value, axis, [(0, 1)])
    value = value + lax.ppermute(value, axis, [(0, 2), (1, 7)])
    far = lax.ppermute(value, axis, [(2, 4), (7, 5)])
    near = lax.ppermute(value, axis, [(2, 3), (7, 6)])
    return value + far + near


def inner(left, right, precision=HIGHEST):
    return lax.dot_general(
        left, right, (((0,), (0,)), ((), ())),
        precision=precision, preferred_element_type=jnp.float32,
    )


def mm(left, right):
    return jnp.dot(left, right, precision=HIGHEST, preferred_element_type=jnp.float32)


def lower_inverse(block):
    eye = jnp.eye(block.shape[0], dtype=block.dtype)
    return lax.linalg.triangular_solve(block, eye, left_side=True, lower=True)


def inverse_factor(gram):
    half = gram.shape[0] // 2
    l11 = lax.linalg.cholesky(gram[:half, :half], symmetrize_input=False)
    i11 = lower_inverse(l11)
    l21 = lax.dot_general(
        gram[half:, :half], i11, (((1,), (1,)), ((), ())),
        precision=HIGHEST, preferred_element_type=jnp.float32,
    )
    schur = gram[half:, half:] - lax.dot_general(
        l21, l21, (((1,), (1,)), ((), ())),
        precision=HIGHEST, preferred_element_type=jnp.float32,
    )
    l22 = lax.linalg.cholesky(schur, symmetrize_input=False)
    i22 = lower_inverse(l22)
    i21 = -mm(mm(i22, l21), i11)
    zeros = jnp.zeros((half, gram.shape[0] - half), gram.dtype)
    return jnp.concatenate(
        [jnp.concatenate([i11, zeros], axis=1), jnp.concatenate([i21, i22], axis=1)], axis=0
    )


def body(block, nrow, ncol):
    cols_here = block.shape[1]
    own = block[:, :NB]
    if ncol == 8:
        panel = tree_broadcast(own, "pcol")
        gram = tree_broadcast(a2a_allreduce(inner(own, own, HIGH), "prow", nrow), "pcol")
    else:
        gram = a2a_allreduce(inner(own, own), "prow", nrow)
        got = a2a_broadcast(jnp.concatenate([own, gram], axis=0), "pcol", ncol)
        panel, gram = got[: own.shape[0]], got[own.shape[0]:]
    inv = inverse_factor(gram)
    products = a2a_allreduce(inner(panel, block, HIGH), "prow", nrow)
    top = mm(inv, products)
    basis = lax.dot_general(
        panel, inv, (((1,), (1,)), ((), ())),
        precision=HIGH, preferred_element_type=jnp.float32,
    )
    rest = block - jnp.dot(basis, top, precision=HIGH, preferred_element_type=jnp.float32)
    widened = jnp.pad(basis, ((0, 0), (0, cols_here - NB)))
    column_ids = lax.axis_index("pcol") * cols_here + jnp.arange(cols_here, dtype=jnp.int32)
    updated = jnp.where((column_ids < NB)[None, :], widened, rest)
    return (top, updated)


def solution(mesh):
    nrow, ncol = mesh.shape["prow"], mesh.shape["pcol"]
    placed = (P("prow", "pcol"),)
    return jax.shard_map(
        lambda b: body(b, nrow, ncol),
        mesh=mesh,
        in_specs=placed,
        out_specs=(P(None, "pcol"), P("prow", "pcol")),
        check_vma=False,
    )
```

```python
import jax
import jax.numpy as jnp
from jax import lax
from jax.sharding import PartitionSpec as P

NB = 256
HIGHEST = lax.Precision.HIGHEST
HIGH = lax.Precision.HIGH


def a2a_allreduce(value, axis, size):
    rows = value.shape[0]
    pieces = value.reshape(size, rows // size, *value.shape[1:])
    mine = lax.all_to_all(pieces, axis, 0, 0).sum(0)
    spread = jnp.broadcast_to(mine[None], (size,) + mine.shape)
    return lax.all_to_all(spread, axis, 0, 0).reshape(value.shape)


def a2a_broadcast(value, axis, size):
    rows = value.shape[0]
    pieces = value.reshape(size, rows // size, *value.shape[1:])
    mine = lax.all_to_all(pieces, axis, 0, 0)[0]
    spread = jnp.broadcast_to(mine[None], (size,) + mine.shape)
    return lax.all_to_all(spread, axis, 0, 0).reshape(value.shape)


def tree_broadcast(value, axis, after=(None, None)):
    me = lax.axis_index(axis)
    source = me == 0
    if after[0] is not None:
        source = source & jnp.isfinite(after[0])
    value = jnp.where(source, value, 0).astype(value.dtype)
    value = value + sum(lax.ppermute(value, axis, [(0, peer)]) for peer in (1, 2, 6))
    if after[1] is not None:
        value = jnp.where(jnp.isfinite(after[1]), value, 0).astype(value.dtype)
    far = lax.ppermute(value, axis, [(2, 4), (6, 5)])
    near = lax.ppermute(value, axis, [(2, 3), (6, 7)])
    return value + far + near


def inner(left, right, precision=HIGHEST):
    return lax.dot_general(
        left, right, (((0,), (0,)), ((), ())),
        precision=precision, preferred_element_type=jnp.float32,
    )


def mm(left, right):
    return jnp.dot(left, right, precision=HIGHEST, preferred_element_type=jnp.float32)


def lower_inverse(block):
    eye = jnp.eye(block.shape[0], dtype=block.dtype)
    return lax.linalg.triangular_solve(block, eye, left_side=True, lower=True)


def inverse_factor(gram):
    half = gram.shape[0] // 2
    l11 = lax.linalg.cholesky(gram[:half, :half], symmetrize_input=False)
    i11 = lower_inverse(l11)
    l21 = lax.dot_general(
        gram[half:, :half], i11, (((1,), (1,)), ((), ())),
        precision=HIGHEST, preferred_element_type=jnp.float32,
    )
    schur = gram[half:, half:] - lax.dot_general(
        l21, l21, (((1,), (1,)), ((), ())),
        precision=HIGHEST, preferred_element_type=jnp.float32,
    )
    l22 = lax.linalg.cholesky(schur, symmetrize_input=False)
    i22 = lower_inverse(l22)
    i21 = -mm(mm(i22, l21), i11)
    zeros = jnp.zeros((half, gram.shape[0] - half), gram.dtype)
    return jnp.concatenate(
        [jnp.concatenate([i11, zeros], axis=1), jnp.concatenate([i21, i22], axis=1)], axis=0
    )


def body(block, nrow, ncol):
    cols_here = block.shape[1]
    own = block[:, :NB]
    if ncol == 8:
        gram = inner(own, own, HIGH)
        full = tree_broadcast(a2a_allreduce(gram, "prow", nrow), "pcol")
        panel = tree_broadcast(own, "pcol", (gram[0, 0], full[0, 0]))
        gram = full
    else:
        gram = a2a_allreduce(inner(own, own), "prow", nrow)
        got = a2a_broadcast(jnp.concatenate([own, gram], axis=0), "pcol", ncol)
        panel, gram = got[: own.shape[0]], got[own.shape[0]:]
    inv = inverse_factor(gram)
    products = a2a_allreduce(inner(panel, block, HIGH), "prow", nrow)
    top = mm(inv, products)
    basis = lax.dot_general(
        panel, inv, (((1,), (1,)), ((), ())),
        precision=HIGH, preferred_element_type=jnp.float32,
    )
    rest = block - jnp.dot(basis, top, precision=HIGH, preferred_element_type=jnp.float32)
    widened = jnp.pad(basis, ((0, 0), (0, cols_here - NB)))
    column_ids = lax.axis_index("pcol") * cols_here + jnp.arange(cols_here, dtype=jnp.int32)
    updated = jnp.where((column_ids < NB)[None, :], widened, rest)
    return (top, updated)


def solution(mesh):
    nrow, ncol = mesh.shape["prow"], mesh.shape["pcol"]
    placed = (P("prow", "pcol"),)
    return jax.shard_map(
        lambda b: body(b, nrow, ncol),
        mesh=mesh,
        in_specs=placed,
        out_specs=(P(None, "pcol"), P("prow", "pcol")),
        check_vma=False,
    )
```

```python
import jax
import jax.numpy as jnp
from jax import lax
from jax.sharding import PartitionSpec as P

NB = 256
HIGHEST = lax.Precision.HIGHEST
HIGH = lax.Precision.HIGH


def a2a_scatter_sum(value, axis, size):
    rows = value.shape[0]
    pieces = value.reshape(size, rows // size, *value.shape[1:])
    return lax.all_to_all(pieces, axis, 0, 0).sum(0)


def a2a_gather(mine, axis, size):
    spread = jnp.broadcast_to(mine[None], (size,) + mine.shape)
    return lax.all_to_all(spread, axis, 0, 0).reshape(size * mine.shape[0], *mine.shape[1:])


def a2a_allreduce(value, axis, size):
    return a2a_gather(a2a_scatter_sum(value, axis, size), axis, size)


def a2a_broadcast(value, axis, size):
    rows = value.shape[0]
    pieces = value.reshape(size, rows // size, *value.shape[1:])
    mine = lax.all_to_all(pieces, axis, 0, 0)[0]
    spread = jnp.broadcast_to(mine[None], (size,) + mine.shape)
    return lax.all_to_all(spread, axis, 0, 0).reshape(value.shape)


def tree_broadcast(value, axis, after=(None, None)):
    me = lax.axis_index(axis)
    value = jnp.where(me == 0, value, 0).astype(value.dtype)
    value = value + lax.ppermute(value, axis, [(0, 1)])
    if after[0] is not None:
        value = jnp.where(jnp.isfinite(after[0]), value, 0).astype(value.dtype)
    value = value + lax.ppermute(value, axis, [(0, 2), (1, 7)])
    if after[1] is not None:
        value = jnp.where(jnp.isfinite(after[1]), value, 0).astype(value.dtype)
    far = lax.ppermute(value, axis, [(2, 4), (7, 5)])
    near = lax.ppermute(value, axis, [(2, 3), (7, 6)])
    return value + far + near


def tree_broadcast_wide(value, axis):
    me = lax.axis_index(axis)
    value = jnp.where(me == 0, value, 0).astype(value.dtype)
    value = value + sum(lax.ppermute(value, axis, [(0, peer)]) for peer in (1, 2, 6))
    far = lax.ppermute(value, axis, [(2, 4), (6, 5)])
    near = lax.ppermute(value, axis, [(2, 3), (6, 7)])
    return value + far + near


def inner(left, right, precision=HIGHEST):
    return lax.dot_general(
        left, right, (((0,), (0,)), ((), ())),
        precision=precision, preferred_element_type=jnp.float32,
    )


def mm(left, right):
    return jnp.dot(left, right, precision=HIGHEST, preferred_element_type=jnp.float32)


def lower_inverse(block):
    eye = jnp.eye(block.shape[0], dtype=block.dtype)
    return lax.linalg.triangular_solve(block, eye, left_side=True, lower=True)


def inverse_factor(gram):
    half = gram.shape[0] // 2
    l11 = lax.linalg.cholesky(gram[:half, :half], symmetrize_input=False)
    i11 = lower_inverse(l11)
    l21 = lax.dot_general(
        gram[half:, :half], i11, (((1,), (1,)), ((), ())),
        precision=HIGHEST, preferred_element_type=jnp.float32,
    )
    schur = gram[half:, half:] - lax.dot_general(
        l21, l21, (((1,), (1,)), ((), ())),
        precision=HIGHEST, preferred_element_type=jnp.float32,
    )
    l22 = lax.linalg.cholesky(schur, symmetrize_input=False)
    i22 = lower_inverse(l22)
    i21 = -mm(mm(i22, l21), i11)
    zeros = jnp.zeros((half, gram.shape[0] - half), gram.dtype)
    return jnp.concatenate(
        [jnp.concatenate([i11, zeros], axis=1), jnp.concatenate([i21, i22], axis=1)], axis=0
    )


def body(block, nrow, ncol):
    cols_here = block.shape[1]
    own = block[:, :NB]
    if ncol == 8:
        gram = inner(own, own, HIGH)
        mine = a2a_scatter_sum(gram, "prow", nrow)
        panel = tree_broadcast(own, "pcol", (gram[0, 0], mine[0, 0]))
        gram = tree_broadcast_wide(a2a_gather(mine, "prow", nrow), "pcol")
    else:
        gram = a2a_allreduce(inner(own, own), "prow", nrow)
        got = a2a_broadcast(jnp.concatenate([own, gram], axis=0), "pcol", ncol)
        panel, gram = got[: own.shape[0]], got[own.shape[0]:]
    inv = inverse_factor(gram)
    products = a2a_allreduce(inner(panel, block, HIGH), "prow", nrow)
    top = mm(inv, products)
    basis = lax.dot_general(
        panel, inv, (((1,), (1,)), ((), ())),
        precision=HIGH, preferred_element_type=jnp.float32,
    )
    rest = block - jnp.dot(basis, top, precision=HIGH, preferred_element_type=jnp.float32)
    widened = jnp.pad(basis, ((0, 0), (0, cols_here - NB)))
    column_ids = lax.axis_index("pcol") * cols_here + jnp.arange(cols_here, dtype=jnp.int32)
    updated = jnp.where((column_ids < NB)[None, :], widened, rest)
    return (top, updated)


def solution(mesh):
    nrow, ncol = mesh.shape["prow"], mesh.shape["pcol"]
    placed = (P("prow", "pcol"),)
    return jax.shard_map(
        lambda b: body(b, nrow, ncol),
        mesh=mesh,
        in_specs=placed,
        out_specs=(P(None, "pcol"), P("prow", "pcol")),
        check_vma=False,
    )
```
